128 devices in a mesh: gx: 8 (over x, y_hi), gy: 16 (over z, y_lo, core).
Axes of the slice: x: 4, y: 4 (y_hi: 2, y_lo: 2; y = y_hi * 2 + y_lo), z: 4, core: 2. Of those that a mesh axis runs over, the one named last changes fastest.
Arguments:
- picture_embeds: bfloat16 [131072, 1152], P(('gx', 'gy')), may hold values from -6 to 6
- motion_embeds: bfloat16 [131072, 1152], P(('gx', 'gy')), may hold values from -6 to 6
- match_indices: int32 [128, 1024], P(('gx', 'gy')), may hold values from 0 to 1023, each once within a row
- sharpness_coefficient: float32 [1], replicated, may hold values from 0.04 to 0.12
- additive_shift: float32 [1], replicated, may hold values from -3 to -1
- precision_gain: float32 [1], replicated, may hold values from 65536 to 262144
Outputs:
- grad_image: bfloat16 [131072, 1152], P(('gx', 'gy'))
- grad_sensor: bfloat16 [131072, 1152], P(('gx', 'gy'))
The draws below stay inside these ranges and needn't reach their ends.
Inputs may be any that keep to these rules, and one draw needn't show every extreme that they name: Each row of match_indices is a permutation of 0 to 1023.
All inputs are finite; a program needn't handle non-finite values.
Results may differ from the reference program's by a relative error of at most 0.0038.
Values may be sent and summed in bfloat16 or wider, within the bound.
No kernel may reach another device: no remote copies, remote signals or barrier semaphores. Data moves between devices by JAX's collectives and lax.ppermute only.
A program may use at most 128 MiB of HBM per device.

```python
import math
import jax
import jax.numpy as jnp
from jax import lax

D = 1152
TILE_HEIGHT = 1024
BLOCKS = 128
TOTAL = 131072


def shard_levels(own_key, shape, cuts, low, high):
    gain = 1.0
    for dim, shards_of in cuts:
        steps = jax.random.uniform(jax.random.fold_in(jax.random.fold_in(own_key, 6), dim), (shards_of,), jnp.float32, low / len(cuts), high / len(cuts))
        gain = gain * jnp.repeat(jnp.exp(steps), shape[dim] // shards_of).reshape((-1,) + (1,) * (len(shape) - 1 - dim))
    return gain


def bell_draw(stream_key, dims, deviation, reach, shards=(), kind=jnp.bfloat16):
    values = jax.random.normal(stream_key, dims, jnp.float32) * deviation
    if len(shards) > 0:
        values = shard_levels(stream_key, dims, shards, -0.22, 0.18) * values
    return jnp.clip(values, min=-reach, max=reach).astype(kind)


def setup_inputs(seed: int = 0) -> dict:
    splits = jax.random.split(jax.random.key(seed), 7)
    picture_embeds = bell_draw(splits[0], (TOTAL, D), 1.0, 6.0, ((0, 128),))
    motion_embeds = bell_draw(splits[1], (TOTAL, D), 1.0, 6.0, ((0, 128),))
    match_indices = jax.vmap(lambda own: jax.random.permutation(own, TILE_HEIGHT))(jax.random.split(splits[2], BLOCKS)).reshape((BLOCKS, TILE_HEIGHT)).astype(jnp.int32)
    sharpness_coefficient = jnp.clip(jax.random.uniform(splits[3], (1,), jnp.float32, 0.04, 0.12), 0.04, 0.12)
    additive_shift = jnp.clip(jax.random.uniform(splits[4], (1,), jnp.float32, -3.0, -1.0), -3.0, -1.0)
    precision_gain = jnp.clip(jnp.exp(jax.random.uniform(splits[5], (1,), jnp.float32, math.log(65536.0), math.log(262144.0))), 65536.0, 262144.0)
    return {"picture_embeds": picture_embeds, "motion_embeds": motion_embeds, "match_indices": match_indices, "sharpness_coefficient": sharpness_coefficient, "additive_shift": additive_shift, "precision_gain": precision_gain}


window_offsets = (-1, 0, 1, 2)


def reference(picture_embeds, motion_embeds, match_indices, sharpness_coefficient, additive_shift, precision_gain):
    tile_total = match_indices.shape[0]
    width = picture_embeds.shape[1]
    picture_tile = picture_embeds.reshape(tile_total, TILE_HEIGHT, width).astype(jnp.float32)
    sensors = motion_embeds.reshape(tile_total, TILE_HEIGHT, width).astype(jnp.float32)
    objective_coefficient = precision_gain[0] * sharpness_coefficient[0] / (tile_total * TILE_HEIGHT)
    columns = jnp.arange(TILE_HEIGHT, dtype=jnp.int32)
    match_target = (match_indices[:, :, None] == columns[None, None, :]).astype(jnp.float32)
    grad_img = jnp.zeros(picture_tile.shape, jnp.float32)
    grad_sen = jnp.zeros(picture_tile.shape, jnp.float32)
    for offset in window_offsets:
        companion_tile = jnp.roll(sensors, -offset, axis=0)
        similarity_grid = sharpness_coefficient[0] * jnp.einsum('wrn,wun->wru', picture_tile, companion_tile) + additive_shift[0]
        logistic_derivative = jax.nn.sigmoid(similarity_grid)
        if offset == 0:
            logistic_derivative = logistic_derivative - match_target
        rounded = lax.optimization_barrier((objective_coefficient * logistic_derivative).astype(jnp.bfloat16))
        weights = rounded.astype(jnp.float32)
        grad_img = grad_img + jnp.einsum('prc,pcd->prd', weights, companion_tile)
        terms = jnp.einsum('prc,prd->pcd', weights, picture_tile)
        grad_sen = grad_sen + jnp.roll(terms, offset, axis=0)
    grad_image = grad_img.reshape(tile_total * TILE_HEIGHT, width).astype(jnp.bfloat16)
    grad_sensor = grad_sen.reshape(tile_total * TILE_HEIGHT, width).astype(jnp.bfloat16)
    return (grad_image, grad_sensor)
```

```python
import jax
import jax.numpy as jnp
from jax import lax
from jax.sharding import PartitionSpec as P


RING = ("gx", "gy")


def shifted(value, by):
    devices = lax.axis_size(RING)
    return lax.ppermute(value, RING, [(i, (i + by) % devices) for i in range(devices)])


def pairing_weights(rows, cols, sharpness_coefficient, additive_shift, objective_coefficient, match_target):
    similarity_grid = lax.dot_general(
        rows, cols, (((1,), (1,)), ((), ())), preferred_element_type=jnp.float32
    )
    logistic_derivative = jax.nn.sigmoid(sharpness_coefficient[0] * similarity_grid + additive_shift[0])
    if match_target is not None:
        logistic_derivative = logistic_derivative - match_target
    return (objective_coefficient * logistic_derivative).astype(jnp.bfloat16)


def apply_rows(weights, entries):
    return jnp.dot(weights, entries, preferred_element_type=jnp.float32)


def apply_cols(weights, entries):
    return lax.dot_general(
        weights, entries, (((0,), (0,)), ((), ())), preferred_element_type=jnp.float32
    )


def per_device(picture_embeds, motion_embeds, match_indices, sharpness_coefficient, additive_shift, precision_gain):
    row_count = picture_embeds.shape[0]
    entire_height = row_count * lax.axis_size(RING)
    objective_coefficient = precision_gain[0] * sharpness_coefficient[0] / entire_height
    columns = jnp.arange(row_count, dtype=jnp.int32)
    match_target = (match_indices[0][:, None] == columns[None, :]).astype(jnp.float32)

    motion_next = shifted(motion_embeds, -1)
    picture_prev = shifted(picture_embeds, 1)
    motion_prev = shifted(motion_embeds, 1)
    picture_next = shifted(picture_embeds, -1)
    motion_next2 = shifted(motion_next, -1)
    picture_prev2 = shifted(picture_prev, 1)

    def weights_of(rows, cols, target=None):
        return pairing_weights(rows, cols, sharpness_coefficient, additive_shift, objective_coefficient, target)

    local_weights = weights_of(picture_embeds, motion_embeds, match_target)
    grad_img = apply_rows(local_weights, motion_embeds)
    grad_sen = apply_cols(local_weights, picture_embeds)

    grad_img = grad_img + apply_rows(weights_of(picture_embeds, motion_prev), motion_prev)
    grad_sen = grad_sen + apply_cols(weights_of(picture_prev, motion_embeds), picture_prev)
    grad_img = grad_img + apply_rows(weights_of(picture_embeds, motion_next), motion_next)
    grad_sen = grad_sen + apply_cols(weights_of(picture_next, motion_embeds), picture_next)
    grad_img = grad_img + apply_rows(weights_of(picture_embeds, motion_next2), motion_next2)
    grad_sen = grad_sen + apply_cols(weights_of(picture_prev2, motion_embeds), picture_prev2)
    return (grad_img.astype(jnp.bfloat16), grad_sen.astype(jnp.bfloat16))


def solution(mesh):
    return jax.shard_map(
        per_device,
        mesh=mesh,
        in_specs=(P(RING, None), P(RING, None), P(RING, None), P(), P(), P()),
        out_specs=(P(RING, None), P(RING, None)),
        check_vma=False,
    )
```

```python
import jax
import jax.numpy as jnp
from jax import lax
from jax.sharding import PartitionSpec as P


RING = ("gx", "gy")


def shifted(value, by):
    devices = lax.axis_size(RING)
    return lax.ppermute(value, RING, [(i, (i + by) % devices) for i in range(devices)])


def pairing_weights(rows, cols, sharpness_coefficient, additive_shift, objective_coefficient, match_target):
    similarity_grid = lax.dot_general(
        rows, cols, (((1,), (1,)), ((), ())), preferred_element_type=jnp.float32
    )
    logistic_derivative = jax.nn.sigmoid(sharpness_coefficient[0] * similarity_grid + additive_shift[0])
    if match_target is not None:
        logistic_derivative = logistic_derivative - match_target
    return (objective_coefficient * logistic_derivative).astype(jnp.bfloat16)


def apply_rows(weights, entries):
    return jnp.dot(weights, entries, preferred_element_type=jnp.float32)


def apply_cols(weights, entries):
    return lax.dot_general(
        weights, entries, (((0,), (0,)), ((), ())), preferred_element_type=jnp.float32
    )


def per_device(picture_embeds, motion_embeds, match_indices, sharpness_coefficient, additive_shift, precision_gain):
    row_count = picture_embeds.shape[0]
    entire_height = row_count * lax.axis_size(RING)
    objective_coefficient = precision_gain[0] * sharpness_coefficient[0] / entire_height
    columns = jnp.arange(row_count, dtype=jnp.int32)
    match_target = (match_indices[0][:, None] == columns[None, :]).astype(jnp.float32)

    devices = lax.axis_size(RING)
    odd = lax.axis_index(RING) % 2 == 1
    motion_next = shifted(motion_embeds, -1)
    picture_prev = shifted(picture_embeds, 1)
    motion_far = lax.ppermute(motion_embeds, RING, [(i, (i - 2) % devices) for i in range(1, devices, 2)])
    picture_far = lax.ppermute(picture_embeds, RING, [(i, (i + 2) % devices) for i in range(0, devices, 2)])
    motion_prev = shifted(motion_embeds, 1)
    picture_next = shifted(picture_embeds, -1)
    motion_relay = lax.ppermute(motion_next, RING, [(i, i - 1) for i in range(1, devices, 2)])
    picture_relay = lax.ppermute(picture_prev, RING, [(i, i + 1) for i in range(0, devices, 2)])
    motion_next2 = jnp.where(odd, motion_far, motion_relay)
    picture_prev2 = jnp.where(odd, picture_relay, picture_far)

    def weights_of(rows, cols, target=None):
        return pairing_weights(rows, cols, sharpness_coefficient, additive_shift, objective_coefficient, target)

    local_weights = weights_of(picture_embeds, motion_embeds, match_target)
    grad_img = apply_rows(local_weights, motion_embeds)
    grad_sen = apply_cols(local_weights, picture_embeds)

    grad_img = grad_img + apply_rows(weights_of(picture_embeds, motion_prev), motion_prev)
    grad_sen = grad_sen + apply_cols(weights_of(picture_prev, motion_embeds), picture_prev)
    grad_img = grad_img + apply_rows(weights_of(picture_embeds, motion_next), motion_next)
    grad_sen = grad_sen + apply_cols(weights_of(picture_next, motion_embeds), picture_next)
    grad_img = grad_img + apply_rows(weights_of(picture_embeds, motion_next2), motion_next2)
    grad_sen = grad_sen + apply_cols(weights_of(picture_prev2, motion_embeds), picture_prev2)
    return (grad_img.astype(jnp.bfloat16), grad_sen.astype(jnp.bfloat16))


def solution(mesh):
    return jax.shard_map(
        per_device,
        mesh=mesh,
        in_specs=(P(RING, None), P(RING, None), P(RING, None), P(), P(), P()),
        out_specs=(P(RING, None), P(RING, None)),
        check_vma=False,
    )
```

```python
import jax
import jax.numpy as jnp
from jax import lax
from jax.sharding import PartitionSpec as P


RING = ("gx", "gy")


def send(value, pairs):
    return lax.ppermute(value, RING, pairs)


def crossing(block, forward, ranges):
    devices = lax.axis_size(RING)
    group = lax.axis_size("gy")
    if forward:
        base = [(i, (i + 1) % devices) for i in range(1, devices, 2)]
        route = lambda k: (4 * k + 3, 4 * k + 7, 4 * k + 4)
    else:
        base = [(i, (i - 1) % devices) for i in range(0, devices, 2)]
        route = lambda k: (4 * k + 4, 4 * k, 4 * k + 3)
    pieces = []
    for lo, hi, ks in ranges:
        part = block[lo:hi]
        hops = [tuple(g + r for r in route(k)) for g in range(0, devices, group) for k in ks]
        starts = {h[0] for h in hops}
        received = send(part, [(s, t) for s, t in base if s not in starts])
        if hops:
            first = send(part, [(h[0], h[1]) for h in hops])
            received = received + send(first, [(h[1], h[2]) for h in hops])
        pieces.append(received)
    return pieces[0] if len(pieces) == 1 else jnp.concatenate(pieces, axis=0)


def pairing_weights(rows, cols, sharpness_coefficient, additive_shift, objective_coefficient, match_target):
    similarity_grid = lax.dot_general(
        rows, cols, (((1,), (1,)), ((), ())), preferred_element_type=jnp.float32
    )
    logistic_derivative = jax.nn.sigmoid(sharpness_coefficient[0] * similarity_grid + additive_shift[0])
    if match_target is not None:
        logistic_derivative = logistic_derivative - match_target
    return (objective_coefficient * logistic_derivative).astype(jnp.bfloat16)


def apply_rows(weights, entries):
    return jnp.dot(weights, entries, preferred_element_type=jnp.float32)


def apply_cols(weights, entries):
    return lax.dot_general(
        weights, entries, (((0,), (0,)), ((), ())), preferred_element_type=jnp.float32
    )


def per_device(picture_embeds, motion_embeds, match_indices, sharpness_coefficient, additive_shift, precision_gain):
    row_count = picture_embeds.shape[0]
    entire_height = row_count * lax.axis_size(RING)
    objective_coefficient = precision_gain[0] * sharpness_coefficient[0] / entire_height
    columns = jnp.arange(row_count, dtype=jnp.int32)
    match_target = (match_indices[0][:, None] == columns[None, :]).astype(jnp.float32)

    devices = lax.axis_size(RING)
    even_to_odd = [(i, i + 1) for i in range(0, devices, 2)]
    odd_to_even = [(i + 1, i) for i in range(0, devices, 2)]
    half = row_count // 2
    motion_from_even = send(motion_embeds, even_to_odd)
    picture_from_even = send(picture_embeds, even_to_odd)
    motion_from_odd = send(motion_embeds, odd_to_even)
    picture_from_odd = send(picture_embeds, odd_to_even)
    fwd_motion = crossing(motion_embeds, True, [(0, row_count, (0, 1, 2))])
    fwd_picture = crossing(picture_embeds, True, [(0, row_count, (1, 2))])
    fwd_picture_prev = crossing(picture_from_even, True, [(0, half, (2,)), (half, row_count, ())])
    bwd_motion = crossing(motion_embeds, False, [(0, row_count, (0, 1, 2))])
    bwd_picture = crossing(picture_embeds, False, [(0, row_count, (0, 1))])
    bwd_motion_next = crossing(motion_from_odd, False, [(0, half, (0,)), (half, row_count, ())])
    motion_relay = send(bwd_motion, odd_to_even)
    picture_relay = send(fwd_picture, even_to_odd)

    motion_prev = fwd_motion + motion_from_even
    picture_prev = fwd_picture + picture_from_even
    picture_prev2 = fwd_picture_prev + picture_relay
    motion_next = bwd_motion + motion_from_odd
    picture_next = bwd_picture + picture_from_odd
    motion_next2 = bwd_motion_next + motion_relay
    motion_prev, picture_prev, picture_prev2 = (lax.optimization_barrier(v) for v in (motion_prev, picture_prev, picture_prev2))
    motion_next, picture_next, motion_next2 = (lax.optimization_barrier(v) for v in (motion_next, picture_next, motion_next2))

    def weights_of(rows, cols, target=None):
        return pairing_weights(rows, cols, sharpness_coefficient, additive_shift, objective_coefficient, target)

    local_weights = weights_of(picture_embeds, motion_embeds, match_target)
    grad_img = apply_rows(local_weights, motion_embeds)
    grad_sen = apply_cols(local_weights, picture_embeds)

    grad_img = grad_img + apply_rows(weights_of(picture_embeds, motion_prev), motion_prev)
    grad_sen = grad_sen + apply_cols(weights_of(picture_prev, motion_embeds), picture_prev)
    grad_img = grad_img + apply_rows(weights_of(picture_embeds, motion_next), motion_next)
    grad_sen = grad_sen + apply_cols(weights_of(picture_next, motion_embeds), picture_next)
    grad_img = grad_img + apply_rows(weights_of(picture_embeds, motion_next2), motion_next2)
    grad_sen = grad_sen + apply_cols(weights_of(picture_prev2, motion_embeds), picture_prev2)
    return (grad_img.astype(jnp.bfloat16), grad_sen.astype(jnp.bfloat16))


def solution(mesh):
    return jax.shard_map(
        per_device,
        mesh=mesh,
        in_specs=(P(RING, None), P(RING, None), P(RING, None), P(), P(), P()),
        out_specs=(P(RING, None), P(RING, None)),
        check_vma=False,
    )
```

```python
import jax
import jax.numpy as jnp
from jax import lax
from jax.sharding import PartitionSpec as P


RING = ("gx", "gy")


def shifted(value, by):
    devices = lax.axis_size(RING)
    return lax.ppermute(value, RING, [(i, (i + by) % devices) for i in range(devices)])


def pairing_weights(rows, cols, sharpness_coefficient, additive_shift, objective_coefficient, match_target):
    similarity_grid = lax.dot_general(
        rows, cols, (((1,), (1,)), ((), ())), preferred_element_type=jnp.float32
    )
    logistic_derivative = jax.nn.sigmoid(sharpness_coefficient[0] * similarity_grid + additive_shift[0])
    if match_target is not None:
        logistic_derivative = logistic_derivative - match_target
    return lax.optimization_barrier((objective_coefficient * logistic_derivative).astype(jnp.bfloat16))


def apply_rows(weights, entries):
    return jnp.dot(weights, entries, preferred_element_type=jnp.float32)


def apply_cols(weights, entries):
    return lax.dot_general(
        weights, entries, (((0,), (0,)), ((), ())), preferred_element_type=jnp.float32
    )


def per_device(picture_embeds, motion_embeds, match_indices, sharpness_coefficient, additive_shift, precision_gain):
    row_count = picture_embeds.shape[0]
    entire_height = row_count * lax.axis_size(RING)
    objective_coefficient = precision_gain[0] * sharpness_coefficient[0] / entire_height
    columns = jnp.arange(row_count, dtype=jnp.int32)
    match_target = (match_indices[0][:, None] == columns[None, :]).astype(jnp.float32)

    motion_next = shifted(motion_embeds, -1)
    picture_prev = shifted(picture_embeds, 1)
    motion_prev = shifted(motion_embeds, 1)
    picture_next = shifted(picture_embeds, -1)
    motion_next2 = shifted(motion_next, -1)
    picture_prev2 = shifted(picture_prev, 1)

    def weights_of(rows, cols, target=None):
        return pairing_weights(rows, cols, sharpness_coefficient, additive_shift, objective_coefficient, target)

    local_weights = weights_of(picture_embeds, motion_embeds, match_target)
    grad_img = apply_rows(local_weights, motion_embeds)
    grad_sen = apply_cols(local_weights, picture_embeds)

    grad_img = grad_img + apply_rows(weights_of(picture_embeds, motion_prev), motion_prev)
    grad_sen = grad_sen + apply_cols(weights_of(picture_prev, motion_embeds), picture_prev)
    grad_img = grad_img + apply_rows(weights_of(picture_embeds, motion_next), motion_next)
    grad_sen = grad_sen + apply_cols(weights_of(picture_next, motion_embeds), picture_next)
    grad_img = grad_img + apply_rows(weights_of(picture_embeds, motion_next2), motion_next2)
    grad_sen = grad_sen + apply_cols(weights_of(picture_prev2, motion_embeds), picture_prev2)
    return (grad_img.astype(jnp.bfloat16), grad_sen.astype(jnp.bfloat16))


def solution(mesh):
    return jax.shard_map(
        per_device,
        mesh=mesh,
        in_specs=(P(RING, None), P(RING, None), P(RING, None), P(), P(), P()),
        out_specs=(P(RING, None), P(RING, None)),
        check_vma=False,
    )
```

```python
import jax
import jax.numpy as jnp
from jax import lax
from jax.sharding import PartitionSpec as P


RING = ("gx", "gy")


def shifted(value, by):
    devices = lax.axis_size(RING)
    return lax.ppermute(value, RING, [(i, (i + by) % devices) for i in range(devices)])


def pairing_weights(rows, cols, sharpness_coefficient, additive_shift, objective_coefficient, match_target):
    similarity_grid = lax.dot_general(
        rows, cols, (((1,), (1,)), ((), ())), preferred_element_type=jnp.float32
    )
    logistic_derivative = jax.nn.sigmoid(sharpness_coefficient[0] * similarity_grid + additive_shift[0])
    if match_target is not None:
        logistic_derivative = logistic_derivative - match_target
    return lax.optimization_barrier((objective_coefficient * logistic_derivative).astype(jnp.bfloat16))


def apply_rows(weights, entries):
    return jnp.dot(weights, entries, preferred_element_type=jnp.float32)


def apply_cols(weights, entries):
    return lax.dot_general(
        weights, entries, (((0,), (0,)), ((), ())), preferred_element_type=jnp.float32
    )


def per_device(picture_embeds, motion_embeds, match_indices, sharpness_coefficient, additive_shift, precision_gain):
    row_count = picture_embeds.shape[0]
    entire_height = row_count * lax.axis_size(RING)
    objective_coefficient = precision_gain[0] * sharpness_coefficient[0] / entire_height
    columns = jnp.arange(row_count, dtype=jnp.int32)
    match_target = (match_indices[0][:, None] == columns[None, :]).astype(jnp.float32)

    motion_next = shifted(motion_embeds, -1)
    picture_prev = shifted(picture_embeds, 1)
    motion_prev = shifted(motion_embeds, 1)
    picture_next = shifted(picture_embeds, -1)
    motion_next2 = shifted(motion_next, -1)
    picture_prev2 = shifted(picture_prev, 1)

    def weights_of(rows, cols, target=None):
        return pairing_weights(rows, cols, sharpness_coefficient, additive_shift, objective_coefficient, target)

    local_weights = weights_of(picture_embeds, motion_embeds, match_target)
    grad_img = lax.optimization_barrier(apply_rows(local_weights, motion_embeds))
    grad_sen = lax.optimization_barrier(apply_cols(local_weights, picture_embeds))

    keep = lax.optimization_barrier
    grad_img = keep(grad_img + apply_rows(weights_of(picture_embeds, motion_next), motion_next))
    grad_sen = keep(grad_sen + apply_cols(weights_of(picture_prev, motion_embeds), picture_prev))
    grad_sen = keep(grad_sen + apply_cols(weights_of(picture_next, motion_embeds), picture_next))
    grad_img = keep(grad_img + apply_rows(weights_of(picture_embeds, motion_prev), motion_prev))
    grad_sen = grad_sen + apply_cols(weights_of(picture_prev2, motion_embeds), picture_prev2)
    grad_img = grad_img + apply_rows(weights_of(picture_embeds, motion_next2), motion_next2)
    return (grad_img.astype(jnp.bfloat16), grad_sen.astype(jnp.bfloat16))


def solution(mesh):
    return jax.shard_map(
        per_device,
        mesh=mesh,
        in_specs=(P(RING, None), P(RING, None), P(RING, None), P(), P(), P()),
        out_specs=(P(RING, None), P(RING, None)),
        check_vma=False,
    )
```

```python
import jax
import jax.numpy as jnp
from jax import lax
from jax.sharding import PartitionSpec as P


RING = ("gx", "gy")


def shifted(value, by):
    devices = lax.axis_size(RING)
    return lax.ppermute(value, RING, [(i, (i + by) % devices) for i in range(devices)])


def pairing_weights(rows, cols, sharpness_coefficient, additive_shift, objective_coefficient, match_target):
    similarity_grid = lax.dot_general(
        rows, cols, (((1,), (1,)), ((), ())), preferred_element_type=jnp.float32
    )
    logistic_derivative = jax.nn.sigmoid(sharpness_coefficient[0] * similarity_grid + additive_shift[0])
    if match_target is not None:
        logistic_derivative = logistic_derivative - match_target
    return lax.optimization_barrier((objective_coefficient * logistic_derivative).astype(jnp.bfloat16))


def apply_rows(weights, entries):
    return jnp.dot(weights, entries, preferred_element_type=jnp.float32)


def apply_cols(weights, entries):
    return lax.dot_general(
        weights, entries, (((0,), (0,)), ((), ())), preferred_element_type=jnp.float32
    )


def per_device(picture_embeds, motion_embeds, match_indices, sharpness_coefficient, additive_shift, precision_gain):
    row_count = picture_embeds.shape[0]
    entire_height = row_count * lax.axis_size(RING)
    objective_coefficient = precision_gain[0] * sharpness_coefficient[0] / entire_height
    columns = jnp.arange(row_count, dtype=jnp.int32)
    match_target = (match_indices[0][:, None] == columns[None, :]).astype(jnp.float32)

    motion_next = shifted(motion_embeds, -1)
    picture_prev = shifted(picture_embeds, 1)
    motion_next2 = shifted(motion_next, -1)
    picture_prev2 = shifted(picture_prev, 1)
    motion_next2, picture_prev2, motion_late, picture_late = lax.optimization_barrier(
        (motion_next2, picture_prev2, motion_embeds, picture_embeds))
    half = row_count // 2
    motion_prev_parts = [shifted(motion_late[:half], 1), shifted(motion_late[half:], 1)]
    picture_next_parts = [shifted(picture_late[:half], -1), shifted(picture_late[half:], -1)]

    def weights_of(rows, cols, target=None):
        return pairing_weights(rows, cols, sharpness_coefficient, additive_shift, objective_coefficient, target)

    local_weights = weights_of(picture_embeds, motion_embeds, match_target)
    grad_img = apply_rows(local_weights, motion_embeds)
    grad_sen = apply_cols(local_weights, picture_embeds)

    grad_img = grad_img + apply_rows(weights_of(picture_embeds, motion_next), motion_next)
    grad_sen = grad_sen + apply_cols(weights_of(picture_prev, motion_embeds), picture_prev)
    grad_img = grad_img + apply_rows(weights_of(picture_embeds, motion_next2), motion_next2)
    grad_sen = grad_sen + apply_cols(weights_of(picture_prev2, motion_embeds), picture_prev2)
    for motion_part, picture_part in zip(motion_prev_parts, picture_next_parts):
        grad_img = grad_img + apply_rows(weights_of(picture_embeds, motion_part), motion_part)
        grad_sen = grad_sen + apply_cols(weights_of(picture_part, motion_embeds), picture_part)
    return (grad_img.astype(jnp.bfloat16), grad_sen.astype(jnp.bfloat16))


def solution(mesh):
    return jax.shard_map(
        per_device,
        mesh=mesh,
        in_specs=(P(RING, None), P(RING, None), P(RING, None), P(), P(), P()),
        out_specs=(P(RING, None), P(RING, None)),
        check_vma=False,
    )
```

```python
import jax
import jax.numpy as jnp
from jax import lax
from jax.sharding import PartitionSpec as P


RING = ("gx", "gy")


def shifted(value, by):
    devices = lax.axis_size(RING)
    return lax.ppermute(value, RING, [(i, (i + by) % devices) for i in range(devices)])


def pairing_weights(rows, cols, sharpness_coefficient, additive_shift, objective_coefficient, match_target):
    similarity_grid = lax.dot_general(
        rows, cols, (((1,), (1,)), ((), ())), preferred_element_type=jnp.float32
    )
    logistic_derivative = jax.nn.sigmoid(sharpness_coefficient[0] * similarity_grid + additive_shift[0])
    if match_target is not None:
        logistic_derivative = logistic_derivative - match_target
    return lax.optimization_barrier((objective_coefficient * logistic_derivative).astype(jnp.bfloat16))


def apply_rows(weights, entries):
    return jnp.dot(weights, entries, preferred_element_type=jnp.float32)


def apply_cols(weights, entries):
    return lax.dot_general(
        weights, entries, (((0,), (0,)), ((), ())), preferred_element_type=jnp.float32
    )


def per_device(picture_embeds, motion_embeds, match_indices, sharpness_coefficient, additive_shift, precision_gain):
    row_count = picture_embeds.shape[0]
    entire_height = row_count * lax.axis_size(RING)
    objective_coefficient = precision_gain[0] * sharpness_coefficient[0] / entire_height
    columns = jnp.arange(row_count, dtype=jnp.int32)
    match_target = (match_indices[0][:, None] == columns[None, :]).astype(jnp.float32)

    motion_next = shifted(motion_embeds, -1)
    picture_prev = shifted(picture_embeds, 1)
    motion_prev = shifted(motion_embeds, 1)
    picture_next = shifted(picture_embeds, -1)
    half = row_count // 2
    motion_next2_parts = [shifted(motion_next[:half], -1), shifted(motion_next[half:], -1)]
    picture_prev2 = shifted(picture_prev, 1)

    def weights_of(rows, cols, target=None):
        return pairing_weights(rows, cols, sharpness_coefficient, additive_shift, objective_coefficient, target)

    local_weights = weights_of(picture_embeds, motion_embeds, match_target)
    grad_img = apply_rows(local_weights, motion_embeds)
    grad_img = grad_img + apply_rows(weights_of(picture_embeds, motion_prev), motion_prev)
    grad_img = grad_img + apply_rows(weights_of(picture_embeds, motion_next), motion_next)
    grad_img = lax.optimization_barrier(grad_img)
    grad_sen = apply_cols(local_weights, picture_embeds)
    grad_sen = grad_sen + apply_cols(weights_of(picture_prev, motion_embeds), picture_prev)
    grad_sen = grad_sen + apply_cols(weights_of(picture_next, motion_embeds), picture_next)
    grad_sen = grad_sen + apply_cols(weights_of(picture_prev2, motion_embeds), picture_prev2)
    grad_sen = grad_sen.astype(jnp.bfloat16)
    for motion_part in motion_next2_parts:
        grad_img = grad_img + apply_rows(weights_of(picture_embeds, motion_part), motion_part)
    return (grad_img.astype(jnp.bfloat16), grad_sen)


def solution(mesh):
    return jax.shard_map(
        per_device,
        mesh=mesh,
        in_specs=(P(RING, None), P(RING, None), P(RING, None), P(), P(), P()),
        out_specs=(P(RING, None), P(RING, None)),
        check_vma=False,
    )
```

```python
import jax
import jax.numpy as jnp
from jax import lax
from jax.sharding import PartitionSpec as P


RING = ("gx", "gy")


def shifted(value, by):
    devices = lax.axis_size(RING)
    return lax.ppermute(value, RING, [(i, (i + by) % devices) for i in range(devices)])


def pairing_weights(rows, cols, sharpness_coefficient, additive_shift, objective_coefficient, match_target):
    similarity_grid = lax.dot_general(
        rows, cols, (((1,), (1,)), ((), ())), preferred_element_type=jnp.float32
    )
    logistic_derivative = jax.nn.sigmoid(sharpness_coefficient[0] * similarity_grid + additive_shift[0])
    if match_target is not None:
        logistic_derivative = logistic_derivative - match_target
    return lax.optimization_barrier((objective_coefficient * logistic_derivative).astype(jnp.bfloat16))


def apply_rows(weights, entries):
    return jnp.dot(weights, entries, preferred_element_type=jnp.float32)


def apply_cols(weights, entries):
    return lax.dot_general(
        weights, entries, (((0,), (0,)), ((), ())), preferred_element_type=jnp.float32
    )


def per_device(picture_embeds, motion_embeds, match_indices, sharpness_coefficient, additive_shift, precision_gain):
    row_count = picture_embeds.shape[0]
    entire_height = row_count * lax.axis_size(RING)
    objective_coefficient = precision_gain[0] * sharpness_coefficient[0] / entire_height
    columns = jnp.arange(row_count, dtype=jnp.int32)
    match_target = (match_indices[0][:, None] == columns[None, :]).astype(jnp.float32)

    stacked = jnp.concatenate([motion_embeds, picture_embeds], axis=0)
    from_prev = shifted(stacked, 1)
    from_next = shifted(stacked, -1)
    motion_prev, picture_prev = from_prev[:row_count], from_prev[row_count:]
    motion_next, picture_next = from_next[:row_count], from_next[row_count:]
    motion_next2 = shifted(motion_next, -1)
    picture_prev2 = shifted(picture_prev, 1)

    def weights_of(rows, cols, target=None):
        return pairing_weights(rows, cols, sharpness_coefficient, additive_shift, objective_coefficient, target)

    local_weights = weights_of(picture_embeds, motion_embeds, match_target)
    grad_img = apply_rows(local_weights, motion_embeds)
    grad_img = grad_img + apply_rows(weights_of(picture_embeds, motion_prev), motion_prev)
    grad_img = grad_img + apply_rows(weights_of(picture_embeds, motion_next), motion_next)
    grad_img = lax.optimization_barrier(grad_img)
    grad_sen = apply_cols(local_weights, picture_embeds)
    grad_sen = grad_sen + apply_cols(weights_of(picture_prev, motion_embeds), picture_prev)
    grad_sen = grad_sen + apply_cols(weights_of(picture_next, motion_embeds), picture_next)
    grad_sen = grad_sen + apply_cols(weights_of(picture_prev2, motion_embeds), picture_prev2)
    grad_sen = grad_sen.astype(jnp.bfloat16)
    grad_img = grad_img + apply_rows(weights_of(picture_embeds, motion_next2), motion_next2)
    return (grad_img.astype(jnp.bfloat16), grad_sen)


def solution(mesh):
    return jax.shard_map(
        per_device,
        mesh=mesh,
        in_specs=(P(RING, None), P(RING, None), P(RING, None), P(), P(), P()),
        out_specs=(P(RING, None), P(RING, None)),
        check_vma=False,
    )
```
